256 devices in a mesh: section: 16 (over z_lo, y), ctx: 8 (over x, core), tp: 2 (over z_hi).
Axes of the slice: x: 4, y: 4, z: 8 (z_hi: 2, z_lo: 4; z = z_hi * 4 + z_lo), core: 2. Of those that a mesh axis runs over, the one named last changes fastest.
Arguments:
- hidden: bfloat16 [16, 3072, 4096], P('section', 'ctx', 'tp'), may hold values from -6 to 6
- norm_gain: bfloat16 [16, 4096], P('section'), may hold values from 0.099609375 to 1.8984375
- w_query: bfloat16 [16, 4096, 4096], P('section', 'ctx', 'tp'), may hold values from -0.125 to 0.125
- w_keyval: bfloat16 [16, 4096, 2, 512], P('section', 'ctx', None, 'tp'), may hold values from -0.125 to 0.125
- prev_tail: bfloat16 [16, 2, 384, 512], P('section', None, None, 'tp'), may hold values from -8 to 8
- glob_kv: bfloat16 [16, 2, 2048, 512], P('section', None, 'ctx', 'tp'), may hold values from -110 to 110
- block_perm: int32 [16, 24], P('section'), may hold values from 0 to 23, as said below
- win_list: int32 [16, 24, 4], P('section'), may hold values from -1 to 26, as said below
- glob_list: int32 [16, 24, 4], P('section'), may hold values from -1 to 15, as said below
Outputs:
- next_hidden: bfloat16 [16, 3072, 4096], P('section', 'ctx', 'tp')
- new_kv: bfloat16 [16, 2, 3072, 512], P('section', None, 'ctx', 'tp')
The draws below stay inside these ranges and needn't reach their ends.
Inputs may be any that keep to these rules, and one draw needn't show every extreme that they name: `block_perm`: each section's row is a permutation of 0 to 23. `win_list`: for logical query block i the first n entries are 3 + i, 2 + i, and so on down by one, for some n from 1 to 4; the rest are -1. `glob_list`: each row holds between 1 and 4 distinct global block ids first, then -1.
All inputs are finite; a program needn't handle non-finite values.
Results may differ from the reference program's by a relative error of at most 0.012.
The reference program's roundings to bfloat16 on the way (of `normed`, `queries`, `table`, `probs` and `layer_out`) count: a program that leaves them out, or rounds other values in their place, can miss the bound.
Values may be sent and summed in bfloat16 or wider, within the bound.
No kernel may reach another device: no remote copies, remote signals or barrier semaphores. Data moves between devices by JAX's collectives and lax.ppermute only.
A program may use at most 128 MiB of HBM per device.

```python
import jax
import jax.numpy as jnp
from jax import lax

D = 4096
H = 32
KVH = 4
HD = 128
BLK = 128
W = 4
G = 4
CB = 24
ROWS = 3072
NG = 16
N_SECTION = 16


def draw_block_perm(key, part):
    section_keys = jax.random.split(key, N_SECTION)
    return jax.vmap(lambda single: jax.random.permutation(single, CB))(section_keys).astype(jnp.int32)


def draw_win_list(key, part):
    lengths = jax.random.randint(jax.random.fold_in(key, 11), (N_SECTION, CB), 1, W + 1)
    lengths = lengths.at[:, CB - 1].set(W)
    offsets = jnp.arange(W, dtype=jnp.int32)
    blocks = jnp.arange(CB, dtype=jnp.int32)
    entries = W - 1 + blocks[:, None] - offsets[None, :]
    listed = jnp.where(offsets[None, None, :] < lengths[:, :, None], entries[None, :, :], -1)
    return listed.astype(jnp.int32)


def draw_glob_list(key, part):
    counts = jax.random.randint(jax.random.fold_in(key, 21), (N_SECTION, CB), 1, G + 1)
    counts = counts.at[:, 0].set(G)
    raw_scores = jax.random.randint(jax.random.fold_in(key, 22), (N_SECTION, CB, NG), 0, 1 << 20)
    distinct = raw_scores * NG + jnp.arange(NG, dtype=jnp.int32)[None, None, :]
    ordering = jnp.argsort(distinct, axis=-1)[:, :, :G].astype(jnp.int32)
    slots = jnp.arange(G, dtype=jnp.int32)
    return jnp.where(slots[None, None, :] < counts[:, :, None], ordering, -1).astype(jnp.int32)


def draw_glob_kv(key, part):
    shape = (N_SECTION, 2, NG * BLK, KVH * HD)
    first_key = jax.random.fold_in(key, 31)
    values = jax.random.normal(first_key, shape, jnp.float32) * 1.4
    return jnp.clip(values, -8.0, 8.0).astype(jnp.bfloat16)


def shard_levels(rng, dims, pieces, low, top_value):
    gain, own = 1.0, jax.random.fold_in(rng, 6)
    for position, blocks in pieces:
        draws = jnp.exp(jax.random.uniform(jax.random.fold_in(own, position), (blocks,), jnp.float32, low / len(pieces), top_value / len(pieces)))
        gain = gain * jnp.repeat(draws, dims[position] // blocks).reshape([-1 if axis == position else 1 for axis in range(len(dims))])
    return gain


def normal_values(key, extent, scale, most, shards=(), kind=jnp.bfloat16):
    values = scale * jax.random.normal(key, extent, jnp.float32)
    if shards:
        values = values * shard_levels(key, extent, shards, -0.22, 0.18)
    return jnp.clip(values, -most, most).astype(kind)


def setup_inputs(seed: int = 0) -> dict:
    seeds = jax.random.split(jax.random.key(seed), 10)
    hidden = normal_values(seeds[0], (N_SECTION, ROWS, D), 1.0, 6.0, ((0, 16), (1, 8), (2, 2)))
    norm_gain = jnp.clip(1.0 + 0.18 * jax.random.normal(seeds[1], (N_SECTION, D), jnp.float32), 0.099609375, 1.8984375).astype(jnp.bfloat16)
    w_query = normal_values(seeds[2], (N_SECTION, D, H * HD), (D // 2) ** -0.5, 0.125, ((0, 16), (1, 8), (2, 2)))
    w_keyval = normal_values(seeds[3], (N_SECTION, D, 2, KVH * HD), (D // 2) ** -0.5, 0.125, ((0, 16), (1, 8), (3, 2)))
    prev_tail = normal_values(seeds[4], (N_SECTION, 2, (W - 1) * BLK, KVH * HD), 1.4, 8.0, ((0, 16), (3, 2)))
    glob_kv = draw_glob_kv(jax.random.fold_in(seeds[9], 71), 0)
    block_perm = draw_block_perm(jax.random.fold_in(seeds[9], 71), 0)
    win_list = draw_win_list(jax.random.fold_in(seeds[9], 71), 0)
    glob_list = draw_glob_list(jax.random.fold_in(seeds[9], 71), 0)
    return dict(hidden=hidden, norm_gain=norm_gain, w_query=w_query, w_keyval=w_keyval, prev_tail=prev_tail, glob_kv=glob_kv, block_perm=block_perm, win_list=win_list, glob_list=glob_list)


epsilon = 1e-05

def section_layer(inputs):
    rows_in, gain_row, query_weight, keyval_weight, tail_kv, global_kv, slot_logical, window_ids, global_ids = inputs
    as_float = rows_in.astype(jnp.float32)
    inv_norm = lax.rsqrt(lax.optimization_barrier(jnp.mean(as_float * as_float, axis=1, keepdims=True)) + epsilon)
    normed = (as_float * inv_norm * gain_row.astype(jnp.float32)).astype(jnp.bfloat16)
    queries = jnp.dot(normed, query_weight, preferred_element_type=jnp.float32).astype(jnp.bfloat16)
    keyvals = jnp.einsum('rd,dck->crk', normed.astype(jnp.float32), keyval_weight.astype(jnp.float32)).astype(jnp.bfloat16)
    kv_width = KVH * HD
    block_index = jnp.arange(CB, dtype=jnp.int32)
    slot_of = lax.optimization_barrier(jnp.sum(block_index[None, :] * (slot_logical[None, :] == block_index[:, None]).astype(jnp.int32), axis=1)).astype(jnp.int32)
    current = keyvals.reshape(2, CB, BLK, kv_width)[:, slot_of]
    table = jnp.concatenate([tail_kv.reshape(2, W - 1, BLK, kv_width), current, global_kv.reshape(2, NG, BLK, kv_width)], axis=1)
    listed = jnp.concatenate([window_ids, jnp.where(global_ids >= 0, global_ids + (W - 1 + CB), -1)], axis=1).astype(jnp.int32)
    listed_slots = listed[slot_logical]
    own_ids = (slot_logical + (W - 1)).astype(jnp.int32)
    q_blocks = queries.reshape(CB, BLK, KVH, H // KVH, HD)
    positions = jnp.arange(BLK, dtype=jnp.int32)

    def one_block(item):
        q_block, block_ids, own_id = item
        safe_ids = jnp.maximum(block_ids, 0)
        key_rows = table[0][safe_ids].reshape((W + G) * BLK, KVH, HD).astype(jnp.float32)
        value_rows = table[1][safe_ids].reshape((W + G) * BLK, KVH, HD).astype(jnp.float32)
        scores = jnp.einsum('qgnd,kgd->gnqk', q_block.astype(jnp.float32), key_rows) * HD ** (-0.5)
        allowed = (block_ids >= 0)[:, None, None] & ((block_ids != own_id)[:, None, None] | (positions[None, None, :] <= positions[None, :, None]))
        allowed = jnp.transpose(allowed, (1, 0, 2)).reshape(BLK, (W + G) * BLK)
        scores = jnp.where(allowed[None, None], scores, -1e+30)
        highest = lax.optimization_barrier(jnp.max(scores, axis=-1, keepdims=True))
        weights = jnp.exp(scores - highest)
        probs = (weights / lax.optimization_barrier(jnp.sum(weights, axis=-1, keepdims=True))).astype(jnp.bfloat16)
        attended = jnp.einsum('gnqk,kgd->qgnd', probs.astype(jnp.float32), value_rows)
        return attended.reshape(BLK, H * HD)
    attended_all = lax.map(one_block, (q_blocks, listed_slots, own_ids)).reshape(CB * BLK, H * HD)
    layer_out = (as_float + attended_all).astype(jnp.bfloat16)
    return (layer_out, keyvals)

def reference(hidden, norm_gain, w_query, w_keyval, prev_tail, glob_kv, block_perm, win_list, glob_list):
    layer_out, new_kv = lax.map(section_layer, (hidden, norm_gain, w_query, w_keyval, prev_tail, glob_kv, block_perm, win_list, glob_list))
    return (jnp.roll(layer_out, 1, axis=0), new_kv)
```

```python
import jax
import jax.numpy as jnp
from jax import lax
from jax.sharding import PartitionSpec as P

HD = 128
BLK = 128
W = 4
G = 4


epsilon = 1e-05


def shifted_2(block, axis, distance):
    devices = range(lax.axis_size(axis))
    route = [((i - distance) % len(devices), i) for i in devices]
    return lax.ppermute(block, axis, route)


def local(
    hidden, norm_gain, w_query, w_keyval, prev_tail, glob_kv, block_perm, win_list, glob_list
):
    own_rows = hidden[0]
    tp_index = lax.axis_index("tp")
    other_rows = shifted_2(own_rows, "tp", 1)
    first_half = jnp.where(tp_index == 0, own_rows, other_rows)
    second_half = jnp.where(tp_index == 0, other_rows, own_rows)
    whole_rows = jnp.concatenate([first_half, second_half], axis=1)
    as_float = whole_rows.astype(jnp.float32)
    inv_norm = lax.rsqrt(jnp.mean(as_float * as_float, axis=1, keepdims=True) + epsilon)
    normed = (as_float * inv_norm * norm_gain[0].astype(jnp.float32)).astype(jnp.bfloat16)
    row_count = normed.shape[0]
    query_width = w_query.shape[2]
    kv_width = w_keyval.shape[3]
    n_ctx = lax.axis_size("ctx")

    own_keyval = w_keyval[0]
    own_global = glob_kv[0]
    packed = jnp.concatenate(
        [own_keyval.reshape(1, -1), own_global.reshape(1, -1)], axis=1
    )
    packed_all = lax.all_gather(packed, "ctx", axis=0, tiled=True)
    full_keyval = packed_all[:, : own_keyval.size].reshape(
        n_ctx * own_keyval.shape[0], 2, kv_width
    )
    global_chunks = packed_all[:, own_keyval.size :].reshape(
        n_ctx, 2, own_global.shape[1] // BLK, BLK, kv_width
    )
    global_blocks = jnp.transpose(global_chunks, (1, 0, 2, 3, 4)).reshape(2, -1, BLK, kv_width)
    global_count = global_blocks.shape[1]

    full_query = lax.all_gather(w_query[0], "ctx", axis=0, tiled=True)
    keyvals = jnp.einsum("rd,dck->crk", normed, full_keyval, preferred_element_type=jnp.float32)
    keyvals = keyvals.astype(jnp.bfloat16)
    queries = jnp.dot(normed, full_query, preferred_element_type=jnp.float32)
    queries = queries.astype(jnp.bfloat16)

    pieces = [keyvals] + [shifted_2(keyvals, "ctx", k) for k in range(1, n_ctx)]
    stacked = jnp.stack(pieces, axis=1)
    tail_blocks = prev_tail[0].reshape(2, W - 1, BLK, kv_width)
    perm_row = block_perm[0]
    stretch_blocks = perm_row.shape[0]
    local_blocks = row_count // BLK
    stack_blocks = stacked.reshape(2, n_ctx * local_blocks, BLK, kv_width)
    my_index = lax.axis_index("ctx")
    my_slots = my_index * local_blocks + jnp.arange(local_blocks, dtype=jnp.int32)
    logical = perm_row[my_slots]
    block_index = jnp.arange(stretch_blocks, dtype=jnp.int32)
    slot_of = jnp.sum(
        block_index[None, :] * (perm_row[None, :] == block_index[:, None]).astype(jnp.int32), axis=1
    )
    stack_pos = ((my_index - slot_of // local_blocks) % n_ctx) * local_blocks + slot_of % local_blocks
    window_ids = win_list[0][logical]
    global_ids = glob_list[0][logical]
    window_mapped = jnp.where(
        window_ids >= W - 1,
        stack_pos[jnp.clip(window_ids - (W - 1), 0, stretch_blocks - 1)] + (W - 1),
        window_ids,
    )
    listed = jnp.concatenate(
        [window_ids, jnp.where(global_ids >= 0, global_ids + (W - 1 + stretch_blocks), -1)], axis=1
    )
    mapped = jnp.concatenate(
        [window_mapped, jnp.where(global_ids >= 0, global_ids + (W - 1 + stretch_blocks), -1)],
        axis=1,
    )
    own_ids = logical + (W - 1)
    table = jnp.concatenate([tail_blocks, stack_blocks, global_blocks], axis=1)
    picked = table[:, jnp.maximum(mapped, 0)]
    span = W + G
    kv_heads = kv_width // HD
    per_group = query_width // HD // kv_heads
    key_rows = picked[0].reshape(local_blocks, span * BLK, kv_heads, HD)
    value_rows = picked[1].reshape(local_blocks, span * BLK, kv_heads, HD)
    query_blocks = queries.reshape(local_blocks, BLK, kv_heads, per_group, HD)
    scores = jnp.einsum(
        "bqgnd,bkgd->bgnqk", query_blocks, key_rows, preferred_element_type=jnp.float32
    ) * HD ** (-0.5)
    positions = jnp.arange(BLK, dtype=jnp.int32)
    allowed = (listed >= 0)[:, :, None, None] & (
        (listed != own_ids[:, None])[:, :, None, None]
        | (positions[None, None, None, :] <= positions[None, None, :, None])
    )
    allowed = jnp.transpose(allowed, (0, 2, 1, 3)).reshape(local_blocks, BLK, span * BLK)
    scores = jnp.where(allowed[:, None, None], scores, -1e30)
    highest = jnp.max(scores, axis=-1, keepdims=True)
    weights = jnp.exp(scores - highest)
    probs = (weights / jnp.sum(weights, axis=-1, keepdims=True)).astype(jnp.bfloat16)
    attended = jnp.einsum(
        "bgnqk,bkgd->bqgnd", probs, value_rows, preferred_element_type=jnp.float32
    )
    attended = attended.reshape(row_count, query_width)
    layer_out = (own_rows.astype(jnp.float32) + attended).astype(jnp.bfloat16)
    shifted = shifted_2(layer_out, "section", 1)
    return (shifted[None], keyvals[None])


def solution(mesh):
    in_specs = (
        P("section", "ctx", "tp"),
        P("section", None),
        P("section", "ctx", "tp"),
        P("section", "ctx", None, "tp"),
        P("section", None, None, "tp"),
        P("section", None, "ctx", "tp"),
        P("section", None),
        P("section", None, None),
        P("section", None, None),
    )
    out_specs = (P("section", "ctx", "tp"), P("section", None, "ctx", "tp"))
    return jax.shard_map(local, mesh=mesh, in_specs=in_specs, out_specs=out_specs, check_vma=False)
```

```python
import jax
import jax.numpy as jnp
from jax import lax
from jax.sharding import PartitionSpec as P

HD = 128
BLK = 128
W = 4
G = 4


epsilon = 1e-05


def shifted_2(block, axis, distance):
    devices = range(lax.axis_size(axis))
    route = [((i - distance) % len(devices), i) for i in devices]
    return lax.ppermute(block, axis, route)


def local(
    hidden, norm_gain, w_query, w_keyval, prev_tail, glob_kv, block_perm, win_list, glob_list
):
    own_rows = hidden[0]
    tp_index = lax.axis_index("tp")
    other_rows = shifted_2(own_rows, "tp", 1)
    first_half = jnp.where(tp_index == 0, own_rows, other_rows)
    second_half = jnp.where(tp_index == 0, other_rows, own_rows)
    whole_rows = jnp.concatenate([first_half, second_half], axis=1)
    as_float = whole_rows.astype(jnp.float32)
    inv_norm = lax.rsqrt(jnp.mean(as_float * as_float, axis=1, keepdims=True) + epsilon)
    normed = (as_float * inv_norm * norm_gain[0].astype(jnp.float32)).astype(jnp.bfloat16)
    row_count = normed.shape[0]
    query_width = w_query.shape[2]
    kv_width = w_keyval.shape[3]
    n_ctx = lax.axis_size("ctx")

    full_keyval = lax.all_gather(w_keyval[0], "ctx", axis=0, tiled=True)
    global_rows = lax.all_gather(glob_kv[0], "ctx", axis=1, tiled=True)
    global_blocks = global_rows.reshape(2, -1, BLK, kv_width)
    own_query, global_blocks = lax.optimization_barrier((w_query[0], global_blocks))
    keyvals = jnp.einsum("rd,dck->crk", normed, full_keyval, preferred_element_type=jnp.float32)
    keyvals = keyvals.astype(jnp.bfloat16)

    pieces = [keyvals] + [shifted_2(keyvals, "ctx", k) for k in range(1, n_ctx)]
    stacked = jnp.stack(pieces, axis=1)
    tail_blocks = prev_tail[0].reshape(2, W - 1, BLK, kv_width)
    perm_row = block_perm[0]
    stretch_blocks = perm_row.shape[0]
    local_blocks = row_count // BLK
    stack_blocks = stacked.reshape(2, n_ctx * local_blocks, BLK, kv_width)
    my_index = lax.axis_index("ctx")
    my_slots = my_index * local_blocks + jnp.arange(local_blocks, dtype=jnp.int32)
    logical = perm_row[my_slots]
    block_index = jnp.arange(stretch_blocks, dtype=jnp.int32)
    slot_of = jnp.sum(
        block_index[None, :] * (perm_row[None, :] == block_index[:, None]).astype(jnp.int32), axis=1
    )
    stack_pos = ((my_index - slot_of // local_blocks) % n_ctx) * local_blocks + slot_of % local_blocks
    window_ids = win_list[0][logical]
    global_ids = glob_list[0][logical]
    window_mapped = jnp.where(
        window_ids >= W - 1,
        stack_pos[jnp.clip(window_ids - (W - 1), 0, stretch_blocks - 1)] + (W - 1),
        window_ids,
    )
    listed = jnp.concatenate(
        [window_ids, jnp.where(global_ids >= 0, global_ids + (W - 1 + stretch_blocks), -1)], axis=1
    )
    mapped = jnp.concatenate(
        [window_mapped, jnp.where(global_ids >= 0, global_ids + (W - 1 + stretch_blocks), -1)],
        axis=1,
    )
    own_ids = logical + (W - 1)
    table = jnp.concatenate([tail_blocks, stack_blocks, global_blocks], axis=1)
    picked = table[:, jnp.maximum(mapped, 0)]
    span = W + G
    kv_heads = kv_width // HD
    per_group = query_width // HD // kv_heads
    key_rows = picked[0].reshape(local_blocks, span * BLK, kv_heads, HD)
    value_rows = picked[1].reshape(local_blocks, span * BLK, kv_heads, HD)
    positions = jnp.arange(BLK, dtype=jnp.int32)
    allowed = (listed >= 0)[:, :, None, None] & (
        (listed != own_ids[:, None])[:, :, None, None]
        | (positions[None, None, None, :] <= positions[None, None, :, None])
    )
    allowed = jnp.transpose(allowed, (0, 2, 1, 3)).reshape(local_blocks, BLK, span * BLK)

    chunk_heads = 4
    chunk_width = chunk_heads * HD
    outputs = []
    for start in range(0, query_width, chunk_width):
        group = start // HD // per_group
        weight_part = lax.all_gather(
            own_query[:, start : start + chunk_width], "ctx", axis=0, tiled=True
        )
        queries = jnp.dot(normed, weight_part, preferred_element_type=jnp.float32)
        queries = queries.astype(jnp.bfloat16).reshape(local_blocks, BLK, chunk_heads, HD)
        scores = jnp.einsum(
            "bqnd,bkd->bnqk", queries, key_rows[:, :, group], preferred_element_type=jnp.float32
        ) * HD ** (-0.5)
        scores = jnp.where(allowed[:, None], scores, -1e30)
        highest = jnp.max(scores, axis=-1, keepdims=True)
        weights = jnp.exp(scores - highest)
        probs = (weights / jnp.sum(weights, axis=-1, keepdims=True)).astype(jnp.bfloat16)
        attended = jnp.einsum(
            "bnqk,bkd->bqnd", probs, value_rows[:, :, group], preferred_element_type=jnp.float32
        )
        attended = attended.reshape(row_count, chunk_width)
        layer_part = (
            own_rows[:, start : start + chunk_width].astype(jnp.float32) + attended
        ).astype(jnp.bfloat16)
        normed, layer_part = lax.optimization_barrier((normed, layer_part))
        outputs.append(shifted_2(layer_part, "section", 1))
    shifted = jnp.concatenate(outputs, axis=1)
    return (shifted[None], keyvals[None])


def solution(mesh):
    in_specs = (
        P("section", "ctx", "tp"),
        P("section", None),
        P("section", "ctx", "tp"),
        P("section", "ctx", None, "tp"),
        P("section", None, None, "tp"),
        P("section", None, "ctx", "tp"),
        P("section", None),
        P("section", None, None),
        P("section", None, None),
    )
    out_specs = (P("section", "ctx", "tp"), P("section", None, "ctx", "tp"))
    return jax.shard_map(local, mesh=mesh, in_specs=in_specs, out_specs=out_specs, check_vma=False)
```
